512 devices in a mesh: dp: 8 (over x, core), expert: 64 (over y, z).
Axes of the slice: x: 4, y: 4, z: 16, core: 2. Of those that a mesh axis runs over, the one named last changes fastest.
Arguments:
- tokens: bfloat16 [65536, 1024], P(('dp', 'expert')), may hold values from -6 to 6
- grad_out: bfloat16 [65536, 1024], P(('dp', 'expert')), may hold values from -6 to 6
- expert_ids: int32 [65536, 8], P(('dp', 'expert')), may hold values from 0 to 63, all different within a row; in each aligned block of 128 rows (0 to 127, 128 to 255, ...) at most 18 rows name the same one
- gates: float32 [65536, 8], P(('dp', 'expert')), may hold values from 0.1 to 0.5
- w_in: bfloat16 [64, 1024, 768], P('expert', 'dp'), may hold values from -0.1875 to 0.1875
- w_down: bfloat16 [64, 384, 1024], P('expert', 'dp'), may hold values from -0.3125 to 0.3125
Outputs:
- grad_tokens: bfloat16 [65536, 1024], P(('dp', 'expert'))
- grad_in: float32 [64, 1024, 768], P('expert', 'dp')
- grad_down: float32 [64, 384, 1024], P('expert', 'dp')
The draws below stay inside these ranges and needn't reach their ends.
Inputs may be any that keep to these rules, and one draw needn't show every extreme that they name: `expert_ids`: each token names 8 different experts; among the tokens of one device no expert is named more than 18 times, a bound that some block reaches.
All inputs are finite; a program needn't handle non-finite values.
Results may differ from the reference program's by a relative error of at most 0.015.
Values may be sent and summed in bfloat16 or wider, within the bound.
No kernel may reach another device: no remote copies, remote signals or barrier semaphores. Data moves between devices by JAX's collectives and lax.ppermute only.
A program may use at most 64 MiB of HBM per device.

```python
import math
import jax
import jax.numpy as jnp
import numpy as np
from jax import lax

D = 1024
H = 384
TOP = 8
TOK_DEV = 128
EXPERTS = 64
CAP = 18
TOKENS = 65536
N_DP = 8
N_EXPERT = 64


def block_levels(stream_key, extent, split, smallest, largest):
    def one(axis_at, parts):
        draws = jax.random.uniform(jax.random.fold_in(jax.random.fold_in(stream_key, 6), axis_at), (parts,), jnp.float32, smallest / len(split), largest / len(split))
        return jnp.repeat(jnp.exp(draws), extent[axis_at] // parts).reshape((-1,) + (1,) * (len(extent) - axis_at - 1))

    level = one(*split[0])
    for cut in split[1:]:
        level = level * one(*cut)
    return level


def routed_block(rng, own, number, rows, amount, top, most, slope):
    ranking = jax.random.permutation(rng, amount)
    packed, ordinary = shares(amount, rows * top, most, slope, True), shares(amount, rows * top, most, slope, False)
    places = jnp.arange(amount)

    def named(sizes, offset_by):
        used = int((sizes > 0).sum())
        fixed = max(1, used // 4)
        passed = fixed + (places - fixed + offset_by * (used - fixed)) % max(1, amount - fixed)
        return jnp.zeros((amount,), jnp.int32).at[ranking[jnp.where(places < fixed, places, passed)]].set(jnp.asarray(sizes, jnp.int32))

    sizes = jnp.where(number % 4 == 0, named(packed, number // 4), named(ordinary, number - number // 4 - 1))
    mixed = jax.random.permutation(jax.random.fold_in(own, 3), amount)
    giver, taker = mixed[0:amount // 2 * 2:2], mixed[1:amount // 2 * 2:2]
    margin = jnp.minimum(sizes[giver] - 1, most - sizes[taker]) // 2
    margin = jnp.where((giver == ranking[0]) | (taker == ranking[0]) | (sizes[taker] == 0), 0, jnp.maximum(margin, 0))
    passed = jax.random.randint(jax.random.fold_in(own, 4), (amount // 2,), 0, 1 << 20) % (margin + 1)
    sizes = sizes.at[giver].add(-passed).at[taker].add(passed)
    labels = jnp.searchsorted(jnp.cumsum(sizes), jnp.arange(rows * top), side="right").astype(jnp.int32)
    listing = labels.reshape(top, rows).T
    listing = listing[jax.random.permutation(jax.random.fold_in(own, 1), rows)]
    offset_by = jax.random.randint(jax.random.fold_in(own, 2), (rows, 1), 0, top)
    return jnp.take_along_axis(listing, (jnp.arange(top)[None, :] + offset_by) % top, axis=1)


def shares(number_of, total, reach, slope, full):
    weights = [(1 << 20) // math.isqrt(rank ** slope) + 1 for rank in range(1, number_of + 1)]
    largest = reach if full else min(reach, max(-(-total // number_of), total * weights[0] // sum(weights)))
    least = 1 if total - largest >= number_of - 1 else 0
    holding, surplus = [largest] + [least] * (number_of - 1), total - largest - least * (number_of - 1)
    while surplus > 0:
        movable = [i for i in range(1, number_of) if holding[i] < largest] or [i for i in range(1, number_of) if holding[i] < reach]
        mass, budget = sum([weights[i] for i in movable]), surplus
        for i in movable:
            addition = min(reach - holding[i], max(1, budget * weights[i] // mass), surplus)
            holding[i] = holding[i] + addition
            surplus = surplus - addition
    return np.array(holding)


def noise(own_key, shape, deviation, bound, pieces=(), held_as=jnp.bfloat16):
    loudness = block_levels(own_key, shape, pieces, -0.22, 0.18) if pieces else 1.0
    values = jax.random.normal(own_key, shape, jnp.float32) * deviation * loudness
    return jnp.minimum(jnp.maximum(values, -bound), bound).astype(held_as)


def setup_inputs(seed: int = 0) -> dict:
    key_list = jax.random.split(jax.random.key(seed), 7)
    tokens = noise(key_list[0], (TOKENS, D), 1.0, 6.0, ((0, 512),))
    grad_out = noise(key_list[1], (TOKENS, D), 0.5, 6.0, ((0, 512),))
    expert_ids_keys = jax.random.split(jax.random.fold_in(key_list[2], 1), TOKENS // TOK_DEV)
    expert_ids_turns = jax.random.permutation(jax.random.fold_in(key_list[2], 3), TOKENS // TOK_DEV)
    expert_ids = jax.vmap(lambda own, number: routed_block(jax.random.fold_in(key_list[2], 2), own, number, TOK_DEV, EXPERTS, TOP, CAP, 2))(expert_ids_keys, expert_ids_turns).reshape((TOKENS, TOP))
    gates = jnp.clip(jnp.exp(math.log(0.5) - 1.609438 * jax.random.uniform(key_list[3], (TOKENS, TOP), jnp.float32) ** block_levels(key_list[3], (TOKENS, TOP), ((0, 512),), -0.2, 0.2)), 0.1, 0.5)
    w_in = noise(key_list[4], (EXPERTS, D, 2 * H), D ** -0.5, 0.1875, ((0, 64), (1, 8)))
    w_down = noise(key_list[5], (EXPERTS, H, D), H ** -0.5, 0.3125, ((0, 64), (1, 8)))
    return dict(tokens=tokens, grad_out=grad_out, expert_ids=expert_ids, gates=gates, w_in=w_in, w_down=w_down)


def hidden_from(preact):
    half_width = preact.shape[1] // 2
    gate_pre = preact[:, :half_width]
    up_pre = preact[:, half_width:]
    sigmoid_gate = jax.nn.sigmoid(gate_pre)
    return (gate_pre * sigmoid_gate * up_pre).astype(jnp.bfloat16)


def pre_grads(preact, grad_hidden):
    half_width = preact.shape[1] // 2
    gate_pre = preact[:, :half_width]
    up_pre = preact[:, half_width:]
    sigmoid_gate = jax.nn.sigmoid(gate_pre)
    grad_gate = grad_hidden * up_pre * sigmoid_gate * (1.0 + gate_pre * (1.0 - sigmoid_gate))
    grad_up = grad_hidden * gate_pre * sigmoid_gate
    return jnp.concatenate([grad_gate, grad_up], axis=1).astype(jnp.bfloat16)


def contract_first(left, right):
    return lax.dot_general(left, right, (((0,), (0,)), ((), ())), preferred_element_type=jnp.float32)


def contract_last(left, right):
    return lax.dot_general(left, right, (((1,), (1,)), ((), ())), preferred_element_type=jnp.float32)


def reference(tokens, grad_out, expert_ids, gates, w_in, w_down):
    block_total = N_DP * N_EXPERT
    route_rows = TOK_DEV * TOP
    route_total = block_total * route_rows
    block_ids = expert_ids.reshape(block_total, route_rows)
    route_marks = (block_ids[:, :, None] == jnp.arange(EXPERTS, dtype=jnp.int32)[None, None, :]).astype(jnp.int32)
    slot_ranks = jnp.sum((jnp.cumsum(route_marks, axis=1) - 1) * route_marks, axis=2)
    block_index = jnp.arange(block_total, dtype=jnp.int32)[:, None]
    targets = ((block_index * EXPERTS + block_ids) * CAP + slot_ranks).reshape(-1).astype(jnp.int32)
    route_index = jnp.arange(route_total, dtype=jnp.int32)
    slot_table = jnp.full((block_total * EXPERTS * CAP,), route_total, jnp.int32).at[targets].set(route_index)
    slot_table = slot_table.reshape(block_total, EXPERTS, CAP).transpose(1, 0, 2).reshape(EXPERTS, block_total * CAP)
    flat_gates = gates.reshape(-1)
    group_rows = N_EXPERT * CAP

    def expert_step(accumulated, inputs):
        slot_routes, weight_first, weight_second = inputs
        occupied = slot_routes < route_total
        clipped = jnp.minimum(slot_routes, route_total - 1)
        source_rows = (clipped // TOP).astype(jnp.int32)
        slot_tokens = jnp.where(occupied[:, None], tokens[source_rows], jnp.zeros((), jnp.bfloat16))
        slot_gates = jnp.where(occupied, flat_gates[clipped], jnp.zeros((), jnp.float32))
        slot_grads = (slot_gates[:, None] * grad_out[source_rows].astype(jnp.float32)).astype(jnp.bfloat16)
        preact = jnp.dot(slot_tokens, weight_first, preferred_element_type=jnp.float32)
        hidden_act = hidden_from(preact)
        grad_hidden = contract_last(slot_grads, weight_second)
        pre_grad = pre_grads(preact, grad_hidden)
        slot_back = contract_last(pre_grad, weight_first).astype(jnp.bfloat16)
        accumulated = accumulated.at[source_rows].add(
            jnp.where(occupied[:, None], slot_back.astype(jnp.float32), jnp.zeros((), jnp.float32)))
        grad_first = jnp.zeros(weight_first.shape, jnp.float32)
        grad_second = jnp.zeros(weight_second.shape, jnp.float32)
        for group_index in range(N_DP):
            lower = group_index * group_rows
            upper = lower + group_rows
            part_first = contract_first(slot_tokens[lower:upper], pre_grad[lower:upper]).astype(jnp.bfloat16)
            part_second = contract_first(hidden_act[lower:upper], slot_grads[lower:upper]).astype(jnp.bfloat16)
            grad_first = grad_first + lax.optimization_barrier(part_first).astype(jnp.float32)
            grad_second = grad_second + lax.optimization_barrier(part_second).astype(jnp.float32)
        return accumulated, (grad_first, grad_second)

    start_value = jnp.zeros((TOKENS, D), jnp.float32)
    accumulated, (grad_in, grad_down) = lax.scan(expert_step, start_value, (slot_table, w_in, w_down))
    return accumulated.astype(jnp.bfloat16), grad_in, grad_down
```

```python
import jax
import jax.numpy as jnp
from jax import lax
from jax.sharding import Mesh
from jax.sharding import PartitionSpec as P


def hidden_from(preact):
    half_width = preact.shape[1] // 2
    gate_pre = preact[:, :half_width]
    up_pre = preact[:, half_width:]
    sigmoid_gate = jax.nn.sigmoid(gate_pre)
    return (gate_pre * sigmoid_gate * up_pre).astype(jnp.bfloat16)


def pre_grads(preact, grad_hidden):
    half_width = preact.shape[1] // 2
    gate_pre = preact[:, :half_width]
    up_pre = preact[:, half_width:]
    sigmoid_gate = jax.nn.sigmoid(gate_pre)
    grad_gate = grad_hidden * up_pre * sigmoid_gate * (1.0 + gate_pre * (1.0 - sigmoid_gate))
    grad_up = grad_hidden * gate_pre * sigmoid_gate
    return jnp.concatenate([grad_gate, grad_up], axis=1).astype(jnp.bfloat16)


def contract_first(left, right):
    return lax.dot_general(
        left, right, (((0,), (0,)), ((), ())), preferred_element_type=jnp.float32
    )


def contract_last(left, right):
    return lax.dot_general(
        left, right, (((1,), (1,)), ((), ())), preferred_element_type=jnp.float32
    )


def expert_exchange(blocks, rows, cols):
    capacity, width = blocks.shape[1], blocks.shape[2]
    blocks = blocks.reshape(rows, cols, capacity, width)
    blocks = lax.all_to_all(blocks, "ez", 1, 1, tiled=True)
    blocks = lax.all_to_all(blocks, "ey", 0, 0, tiled=True)
    return blocks.reshape(rows * cols, capacity, width)


def on_device(tokens, grad_out, expert_ids, gates, w_in, w_down):
    token_rows, model_width = tokens.shape
    route_width = expert_ids.shape[1]
    rows = lax.axis_size("ey")
    cols = lax.axis_size("ez")
    expert_count = rows * cols
    route_total = token_rows * route_width
    capacity = route_total // expert_count + max(1, route_total // (8 * expert_count))
    slot_total = expert_count * capacity
    flat_ids = expert_ids.reshape(route_total)
    route_marks = (flat_ids[:, None] == jnp.arange(expert_count, dtype=jnp.int32)[None, :]).astype(
        jnp.int32
    )
    route_index = jnp.arange(route_total, dtype=jnp.int32)
    lower_table = (route_index[None, :] <= route_index[:, None]).astype(jnp.bfloat16)
    running = jnp.dot(
        lower_table, route_marks.astype(jnp.bfloat16), preferred_element_type=jnp.float32
    )
    slot_ranks = jnp.sum((running.astype(jnp.int32) - 1) * route_marks, axis=1)
    targets = (flat_ids * capacity + slot_ranks).reshape(token_rows, route_width)
    slot_index = jnp.arange(slot_total, dtype=jnp.int32)
    slot_hits = targets[None, :, :] == slot_index[:, None, None]
    slot_of_token = jnp.any(slot_hits, axis=2).astype(jnp.bfloat16)
    slot_gates = jnp.sum(jnp.where(slot_hits, gates[None, :, :], 0.0), axis=(1, 2))
    send_tokens = jnp.dot(slot_of_token, tokens, preferred_element_type=jnp.float32).astype(
        jnp.bfloat16
    )
    picked_grads = jnp.dot(slot_of_token, grad_out, preferred_element_type=jnp.float32)
    send_grads = (slot_gates[:, None] * picked_grads).astype(jnp.bfloat16)
    send_both = jnp.concatenate([send_tokens, send_grads], axis=1)
    recv_both = expert_exchange(
        send_both.reshape(expert_count, capacity, 2 * model_width), rows, cols
    ).reshape(slot_total, 2 * model_width)
    slot_tokens = recv_both[:, :model_width]
    slot_grads = recv_both[:, model_width:]
    local_in = w_in[0]
    local_down = w_down[0]
    full_in, full_down = (
        lax.all_gather(local_in, "dp", axis=0, tiled=True),
        lax.all_gather(local_down, "dp", axis=0, tiled=True),
    )
    preact = jnp.dot(slot_tokens, full_in, preferred_element_type=jnp.float32)
    grad_hidden = contract_last(slot_grads, full_down)
    pre_grad = pre_grads(preact, grad_hidden)
    slot_back = contract_last(pre_grad, full_in).astype(jnp.bfloat16)
    hidden_act = hidden_from(preact)
    grad_in_local = lax.psum_scatter(
        contract_first(slot_tokens, pre_grad).astype(jnp.bfloat16),
        "dp",
        scatter_dimension=0,
        tiled=True,
    ).astype(jnp.float32)
    grad_down_local = lax.psum_scatter(
        contract_first(hidden_act, slot_grads).astype(jnp.bfloat16),
        "dp",
        scatter_dimension=0,
        tiled=True,
    ).astype(jnp.float32)
    slot_return = expert_exchange(
        slot_back.reshape(expert_count, capacity, model_width), rows, cols
    ).reshape(slot_total, model_width)
    grad_tokens = contract_first(slot_of_token, slot_return).astype(jnp.bfloat16)
    return (grad_tokens, grad_in_local[None], grad_down_local[None])


def solution(mesh):
    dp_size = mesh.shape["dp"]
    expert_devices = mesh.devices.reshape(dp_size, -1)
    rows = 4 if expert_devices.shape[1] % 4 == 0 else 1
    split_mesh = Mesh(
        expert_devices.reshape(dp_size, rows, expert_devices.shape[1] // rows),
        ("dp", "ey", "ez"),
    )
    token_spec = P(("dp", "ey", "ez"), None)
    weight_spec = P(("ey", "ez"), "dp", None)
    in_specs = (token_spec, token_spec, token_spec, token_spec, weight_spec, weight_spec)
    out_specs = (token_spec, weight_spec, weight_spec)
    return jax.shard_map(
        on_device, mesh=split_mesh, in_specs=in_specs, out_specs=out_specs, check_vma=False
    )
```

```python
import jax
import jax.numpy as jnp
from jax import lax
from jax.sharding import PartitionSpec as P


def hidden_from(preact):
    half_width = preact.shape[1] // 2
    gate_pre = preact[:, :half_width]
    up_pre = preact[:, half_width:]
    sigmoid_gate = jax.nn.sigmoid(gate_pre)
    return (gate_pre * sigmoid_gate * up_pre).astype(jnp.bfloat16)


def pre_grads(preact, grad_hidden):
    half_width = preact.shape[1] // 2
    gate_pre = preact[:, :half_width]
    up_pre = preact[:, half_width:]
    sigmoid_gate = jax.nn.sigmoid(gate_pre)
    grad_gate = grad_hidden * up_pre * sigmoid_gate * (1.0 + gate_pre * (1.0 - sigmoid_gate))
    grad_up = grad_hidden * gate_pre * sigmoid_gate
    return jnp.concatenate([grad_gate, grad_up], axis=1).astype(jnp.bfloat16)


def contract_first(left, right):
    return lax.dot_general(
        left, right, (((0,), (0,)), ((), ())), preferred_element_type=jnp.float32
    )


def contract_last(left, right):
    return lax.dot_general(
        left, right, (((1,), (1,)), ((), ())), preferred_element_type=jnp.float32
    )


def expert_exchange(slots, expert_count):
    slot_total, width = slots.shape
    blocks = slots.reshape(expert_count, slot_total // expert_count * width // 128, 128)
    blocks = lax.all_to_all(blocks, "expert", 0, 0, tiled=True)
    return blocks.reshape(slot_total, width)


def on_device(tokens, grad_out, expert_ids, gates, w_in, w_down):
    token_rows, model_width = tokens.shape
    route_width = expert_ids.shape[1]
    expert_count = lax.axis_size("expert")
    route_total = token_rows * route_width
    capacity = route_total // expert_count + max(1, route_total // (8 * expert_count))
    slot_total = expert_count * capacity
    flat_ids = expert_ids.reshape(route_total)
    route_marks = (flat_ids[:, None] == jnp.arange(expert_count, dtype=jnp.int32)[None, :]).astype(
        jnp.int32
    )
    route_index = jnp.arange(route_total, dtype=jnp.int32)
    lower_table = (route_index[None, :] <= route_index[:, None]).astype(jnp.bfloat16)
    running = jnp.dot(
        lower_table, route_marks.astype(jnp.bfloat16), preferred_element_type=jnp.float32
    )
    slot_ranks = jnp.sum((running.astype(jnp.int32) - 1) * route_marks, axis=1)
    targets = flat_ids * capacity + slot_ranks
    slot_index = jnp.arange(slot_total, dtype=jnp.int32)
    slot_hits = slot_index[:, None] == targets[None, :]
    slot_gates = jnp.sum(jnp.where(slot_hits, gates.reshape(route_total)[None, :], 0.0), axis=1)
    token_of_route = (
        route_index[:, None] // route_width == jnp.arange(token_rows, dtype=jnp.int32)[None, :]
    ).astype(jnp.bfloat16)
    slot_of_token = jnp.dot(
        slot_hits.astype(jnp.bfloat16), token_of_route, preferred_element_type=jnp.float32
    ).astype(jnp.bfloat16)
    send_tokens = jnp.dot(slot_of_token, tokens, preferred_element_type=jnp.float32).astype(
        jnp.bfloat16
    )
    picked_grads = jnp.dot(slot_of_token, grad_out, preferred_element_type=jnp.float32)
    send_grads = (slot_gates[:, None] * picked_grads).astype(jnp.bfloat16)
    send_both = jnp.concatenate([send_tokens, send_grads], axis=1)
    recv_both = expert_exchange(send_both, expert_count)
    slot_tokens = recv_both[:, :model_width]
    slot_grads = recv_both[:, model_width:]
    local_in = w_in[0]
    local_down = w_down[0]
    full_in, full_down = (
        lax.all_gather(local_in, "dp", axis=0, tiled=True),
        lax.all_gather(local_down, "dp", axis=0, tiled=True),
    )
    preact = jnp.dot(slot_tokens, full_in, preferred_element_type=jnp.float32)
    grad_hidden = contract_last(slot_grads, full_down)
    pre_grad = pre_grads(preact, grad_hidden)
    slot_back = contract_last(pre_grad, full_in).astype(jnp.bfloat16)
    hidden_act = hidden_from(preact)
    grad_in_local = lax.psum_scatter(
        contract_first(slot_tokens, pre_grad).astype(jnp.bfloat16),
        "dp",
        scatter_dimension=0,
        tiled=True,
    ).astype(jnp.float32)
    grad_down_local = lax.psum_scatter(
        contract_first(hidden_act, slot_grads).astype(jnp.bfloat16),
        "dp",
        scatter_dimension=0,
        tiled=True,
    ).astype(jnp.float32)
    slot_return = expert_exchange(slot_back, expert_count)
    grad_tokens = contract_first(slot_of_token, slot_return).astype(jnp.bfloat16)
    return (grad_tokens, grad_in_local[None], grad_down_local[None])


def solution(mesh):
    token_spec = P(("dp", "expert"), None)
    weight_spec = P("expert", "dp", None)
    in_specs = (token_spec, token_spec, token_spec, token_spec, weight_spec, weight_spec)
    out_specs = (token_spec, weight_spec, weight_spec)
    return jax.shard_map(
        on_device, mesh=mesh, in_specs=in_specs, out_specs=out_specs, check_vma=False
    )
```

```python
import jax
import jax.numpy as jnp
from jax import lax
from jax.sharding import PartitionSpec as P


def hidden_from(preact):
    half_width = preact.shape[1] // 2
    gate_pre = preact[:, :half_width]
    up_pre = preact[:, half_width:]
    sigmoid_gate = jax.nn.sigmoid(gate_pre)
    return (gate_pre * sigmoid_gate * up_pre).astype(jnp.bfloat16)


def pre_grads(preact, grad_hidden):
    half_width = preact.shape[1] // 2
    gate_pre = preact[:, :half_width]
    up_pre = preact[:, half_width:]
    sigmoid_gate = jax.nn.sigmoid(gate_pre)
    grad_gate = grad_hidden * up_pre * sigmoid_gate * (1.0 + gate_pre * (1.0 - sigmoid_gate))
    grad_up = grad_hidden * gate_pre * sigmoid_gate
    return jnp.concatenate([grad_gate, grad_up], axis=1).astype(jnp.bfloat16)


def contract_first(left, right):
    return lax.dot_general(
        left, right, (((0,), (0,)), ((), ())), preferred_element_type=jnp.float32
    )


def contract_last(left, right):
    return lax.dot_general(
        left, right, (((1,), (1,)), ((), ())), preferred_element_type=jnp.float32
    )


def expert_exchange(slots, expert_count):
    slot_total, chunks, lanes = slots.shape
    blocks = slots.reshape(expert_count, slot_total // expert_count * chunks, lanes)
    blocks = lax.all_to_all(blocks, "expert", 0, 0, tiled=True)
    return blocks.reshape(slot_total, chunks, lanes)


def on_device(tokens, grad_out, expert_ids, gates, w_in, w_down):
    token_rows, model_width = tokens.shape
    route_width = expert_ids.shape[1]
    expert_count = lax.axis_size("expert")
    route_total = token_rows * route_width
    capacity = route_total // expert_count + max(1, route_total // (8 * expert_count))
    slot_total = expert_count * capacity
    flat_ids = expert_ids.reshape(route_total)
    route_marks = (flat_ids[:, None] == jnp.arange(expert_count, dtype=jnp.int32)[None, :]).astype(
        jnp.int32
    )
    route_index = jnp.arange(route_total, dtype=jnp.int32)
    lower_table = (route_index[None, :] <= route_index[:, None]).astype(jnp.bfloat16)
    running = jnp.dot(
        lower_table, route_marks.astype(jnp.bfloat16), preferred_element_type=jnp.float32
    )
    slot_ranks = jnp.sum((running.astype(jnp.int32) - 1) * route_marks, axis=1)
    targets = flat_ids * capacity + slot_ranks
    slot_index = jnp.arange(slot_total, dtype=jnp.int32)
    slot_hits = slot_index[:, None] == targets[None, :]
    slot_gates = jnp.sum(jnp.where(slot_hits, gates.reshape(route_total)[None, :], 0.0), axis=1)
    token_of_route = (
        route_index[:, None] // route_width == jnp.arange(token_rows, dtype=jnp.int32)[None, :]
    ).astype(jnp.bfloat16)
    slot_of_token = jnp.dot(
        slot_hits.astype(jnp.bfloat16), token_of_route, preferred_element_type=jnp.float32
    ).astype(jnp.bfloat16)
    chunks = model_width // 128
    send_tokens = lax.dot_general(
        slot_of_token,
        tokens.reshape(token_rows, chunks, 128),
        (((1,), (0,)), ((), ())),
        preferred_element_type=jnp.float32,
    ).astype(jnp.bfloat16)
    picked_grads = lax.dot_general(
        slot_of_token,
        grad_out.reshape(token_rows, chunks, 128),
        (((1,), (0,)), ((), ())),
        preferred_element_type=jnp.float32,
    )
    send_grads = (slot_gates[:, None, None] * picked_grads).astype(jnp.bfloat16)
    send_both = jnp.concatenate([send_tokens, send_grads], axis=1)
    recv_both = expert_exchange(send_both, expert_count)
    slot_tokens = recv_both[:, :chunks, :].reshape(slot_total, model_width)
    slot_grads = recv_both[:, chunks:, :].reshape(slot_total, model_width)
    local_in = w_in[0]
    local_down = w_down[0]
    full_in, full_down = (
        lax.all_gather(local_in, "dp", axis=0, tiled=True),
        lax.all_gather(local_down, "dp", axis=0, tiled=True),
    )
    preact = jnp.dot(slot_tokens, full_in, preferred_element_type=jnp.float32)
    grad_hidden = contract_last(slot_grads, full_down)
    pre_grad = pre_grads(preact, grad_hidden)
    slot_back = lax.dot_general(
        pre_grad,
        full_in.reshape(chunks, 128, full_in.shape[1]),
        (((1,), (2,)), ((), ())),
        preferred_element_type=jnp.float32,
    ).astype(jnp.bfloat16)
    hidden_act = hidden_from(preact)
    grad_in_local = lax.psum_scatter(
        contract_first(slot_tokens, pre_grad).astype(jnp.bfloat16),
        "dp",
        scatter_dimension=0,
        tiled=True,
    ).astype(jnp.float32)
    grad_down_local = lax.psum_scatter(
        contract_first(hidden_act, slot_grads).astype(jnp.bfloat16),
        "dp",
        scatter_dimension=0,
        tiled=True,
    ).astype(jnp.float32)
    slot_return = expert_exchange(slot_back, expert_count)
    grad_tokens = (
        contract_first(slot_of_token, slot_return)
        .astype(jnp.bfloat16)
        .reshape(token_rows, model_width)
    )
    return (grad_tokens, grad_in_local[None], grad_down_local[None])


def solution(mesh):
    token_spec = P(("dp", "expert"), None)
    weight_spec = P("expert", "dp", None)
    in_specs = (token_spec, token_spec, token_spec, token_spec, weight_spec, weight_spec)
    out_specs = (token_spec, weight_spec, weight_spec)
    return jax.shard_map(
        on_device, mesh=mesh, in_specs=in_specs, out_specs=out_specs, check_vma=False
    )
```

```python
import jax
import jax.numpy as jnp
from jax import lax
from jax.sharding import PartitionSpec as P


def hidden_from(preact):
    half_width = preact.shape[1] // 2
    gate_pre = preact[:, :half_width]
    up_pre = preact[:, half_width:]
    sigmoid_gate = jax.nn.sigmoid(gate_pre)
    return (gate_pre * sigmoid_gate * up_pre).astype(jnp.bfloat16)


def pre_grads(preact, grad_hidden):
    half_width = preact.shape[1] // 2
    gate_pre = preact[:, :half_width]
    up_pre = preact[:, half_width:]
    sigmoid_gate = jax.nn.sigmoid(gate_pre)
    grad_gate = grad_hidden * up_pre * sigmoid_gate * (1.0 + gate_pre * (1.0 - sigmoid_gate))
    grad_up = grad_hidden * gate_pre * sigmoid_gate
    return jnp.concatenate([grad_gate, grad_up], axis=1).astype(jnp.bfloat16)


def contract_first(left, right):
    return lax.dot_general(
        left, right, (((0,), (0,)), ((), ())), preferred_element_type=jnp.float32
    )


def contract_last(left, right):
    return lax.dot_general(
        left, right, (((1,), (1,)), ((), ())), preferred_element_type=jnp.float32
    )


def expert_exchange(slots, expert_count):
    slot_total, chunks, lanes = slots.shape
    blocks = slots.reshape(expert_count, slot_total // expert_count * chunks, lanes)
    blocks = lax.all_to_all(blocks, "expert", 0, 0, tiled=True)
    return blocks.reshape(slot_total, chunks, lanes)


def on_device(tokens, grad_out, expert_ids, gates, w_in, w_down):
    token_rows, model_width = tokens.shape
    route_width = expert_ids.shape[1]
    expert_count = lax.axis_size("expert")
    route_total = token_rows * route_width
    capacity = route_total // expert_count + max(1, route_total // (8 * expert_count))
    slot_total = expert_count * capacity
    flat_ids = expert_ids.reshape(route_total)
    route_marks = (flat_ids[:, None] == jnp.arange(expert_count, dtype=jnp.int32)[None, :]).astype(
        jnp.int32
    )
    route_index = jnp.arange(route_total, dtype=jnp.int32)
    lower_table = (route_index[None, :] <= route_index[:, None]).astype(jnp.bfloat16)
    running = jnp.dot(
        lower_table, route_marks.astype(jnp.bfloat16), preferred_element_type=jnp.float32
    )
    slot_ranks = jnp.sum((running.astype(jnp.int32) - 1) * route_marks, axis=1)
    targets = flat_ids * capacity + slot_ranks
    slot_index = jnp.arange(slot_total, dtype=jnp.int32)
    slot_hits = slot_index[:, None] == targets[None, :]
    slot_gates = jnp.sum(jnp.where(slot_hits, gates.reshape(route_total)[None, :], 0.0), axis=1)
    token_of_route = (
        route_index[:, None] // route_width == jnp.arange(token_rows, dtype=jnp.int32)[None, :]
    ).astype(jnp.bfloat16)
    slot_of_token = jnp.dot(
        slot_hits.astype(jnp.bfloat16), token_of_route, preferred_element_type=jnp.float32
    ).astype(jnp.bfloat16)
    chunks = model_width // 128
    both_rows = jnp.concatenate(
        [tokens.reshape(token_rows, chunks, 128), grad_out.reshape(token_rows, chunks, 128)],
        axis=1,
    )
    picked = lax.dot_general(
        slot_of_token, both_rows, (((1,), (0,)), ((), ())), preferred_element_type=jnp.float32
    )
    chunk_index = jnp.arange(2 * chunks, dtype=jnp.int32)[None, :, None]
    row_scale = jnp.where(chunk_index < chunks, jnp.ones((), jnp.float32), slot_gates[:, None, None])
    send_both = (row_scale * picked).astype(jnp.bfloat16)
    recv_both = expert_exchange(send_both, expert_count)
    slot_tokens = recv_both[:, :chunks, :].reshape(slot_total, model_width)
    slot_grads = recv_both[:, chunks:, :].reshape(slot_total, model_width)
    local_in = w_in[0]
    local_down = w_down[0]
    full_in, full_down = (
        lax.all_gather(local_in, "dp", axis=0, tiled=True),
        lax.all_gather(local_down, "dp", axis=0, tiled=True),
    )
    preact = jnp.dot(slot_tokens, full_in, preferred_element_type=jnp.float32)
    grad_hidden = contract_last(slot_grads, full_down)
    pre_grad = pre_grads(preact, grad_hidden)
    slot_back = (
        contract_last(pre_grad, full_in).astype(jnp.bfloat16).reshape(slot_total, chunks, 128)
    )
    hidden_act = hidden_from(preact)
    grad_in_local = lax.psum_scatter(
        contract_first(slot_tokens, pre_grad).astype(jnp.bfloat16),
        "dp",
        scatter_dimension=0,
        tiled=True,
    ).astype(jnp.float32)
    grad_down_local = lax.psum_scatter(
        contract_first(hidden_act, slot_grads).astype(jnp.bfloat16),
        "dp",
        scatter_dimension=0,
        tiled=True,
    ).astype(jnp.float32)
    slot_return = expert_exchange(slot_back, expert_count)
    grad_tokens = (
        contract_first(slot_of_token, slot_return)
        .astype(jnp.bfloat16)
        .reshape(token_rows, model_width)
    )
    return (grad_tokens, grad_in_local[None], grad_down_local[None])


def solution(mesh):
    token_spec = P(("dp", "expert"), None)
    weight_spec = P("expert", "dp", None)
    in_specs = (token_spec, token_spec, token_spec, token_spec, weight_spec, weight_spec)
    out_specs = (token_spec, weight_spec, weight_spec)
    return jax.shard_map(
        on_device, mesh=mesh, in_specs=in_specs, out_specs=out_specs, check_vma=False
    )
```

```python
import jax
import jax.numpy as jnp
from jax import lax
from jax.sharding import PartitionSpec as P


def hidden_from(preact):
    half_width = preact.shape[1] // 2
    gate_pre = preact[:, :half_width]
    up_pre = preact[:, half_width:]
    sigmoid_gate = jax.nn.sigmoid(gate_pre)
    return (gate_pre * sigmoid_gate * up_pre).astype(jnp.bfloat16)


def pre_grads(preact, grad_hidden):
    half_width = preact.shape[1] // 2
    gate_pre = preact[:, :half_width]
    up_pre = preact[:, half_width:]
    sigmoid_gate = jax.nn.sigmoid(gate_pre)
    grad_gate = grad_hidden * up_pre * sigmoid_gate * (1.0 + gate_pre * (1.0 - sigmoid_gate))
    grad_up = grad_hidden * gate_pre * sigmoid_gate
    return jnp.concatenate([grad_gate, grad_up], axis=1).astype(jnp.bfloat16)


def contract_first(left, right):
    return lax.dot_general(
        left, right, (((0,), (0,)), ((), ())), preferred_element_type=jnp.float32
    )


def contract_last(left, right):
    return lax.dot_general(
        left, right, (((1,), (1,)), ((), ())), preferred_element_type=jnp.float32
    )


def expert_exchange(slots, expert_count):
    slot_total, chunks, lanes = slots.shape
    blocks = slots.reshape(expert_count, slot_total // expert_count * chunks, lanes)
    blocks = lax.all_to_all(blocks, "expert", 0, 0, tiled=True)
    return blocks.reshape(slot_total, chunks, lanes)


def on_device(tokens, grad_out, expert_ids, gates, w_in, w_down):
    token_rows, model_width = tokens.shape
    route_width = expert_ids.shape[1]
    expert_count = lax.axis_size("expert")
    route_total = token_rows * route_width
    capacity = route_total // expert_count + max(1, route_total // (8 * expert_count))
    slot_total = expert_count * capacity
    flat_ids = expert_ids.reshape(route_total)
    route_marks = (flat_ids[:, None] == jnp.arange(expert_count, dtype=jnp.int32)[None, :]).astype(
        jnp.int32
    )
    route_index = jnp.arange(route_total, dtype=jnp.int32)
    lower_table = (route_index[None, :] <= route_index[:, None]).astype(jnp.bfloat16)
    running = jnp.dot(
        lower_table, route_marks.astype(jnp.bfloat16), preferred_element_type=jnp.float32
    )
    slot_ranks = jnp.sum((running.astype(jnp.int32) - 1) * route_marks, axis=1)
    targets = flat_ids * capacity + slot_ranks
    slot_index = jnp.arange(slot_total, dtype=jnp.int32)
    slot_hits = slot_index[:, None] == targets[None, :]
    slot_gates = jnp.sum(jnp.where(slot_hits, gates.reshape(route_total)[None, :], 0.0), axis=1)
    token_of_route = (
        route_index[:, None] // route_width == jnp.arange(token_rows, dtype=jnp.int32)[None, :]
    ).astype(jnp.bfloat16)
    slot_of_token = jnp.dot(
        slot_hits.astype(jnp.bfloat16), token_of_route, preferred_element_type=jnp.float32
    ).astype(jnp.bfloat16)
    chunks = model_width // 128
    both_rows = jnp.concatenate(
        [tokens.reshape(token_rows, chunks, 128), grad_out.reshape(token_rows, chunks, 128)],
        axis=1,
    )
    slot_routes = jnp.sum(jnp.where(slot_hits, route_index[None, :], 0), axis=1)
    occupied = jnp.any(slot_hits, axis=1)
    picked = both_rows[slot_routes // route_width].astype(jnp.float32)
    chunk_index = jnp.arange(2 * chunks, dtype=jnp.int32)[None, :, None]
    row_scale = jnp.where(chunk_index < chunks, jnp.ones((), jnp.float32), slot_gates[:, None, None])
    row_scale = jnp.where(occupied[:, None, None], row_scale, jnp.zeros((), jnp.float32))
    send_both = (row_scale * picked).astype(jnp.bfloat16)
    recv_both = expert_exchange(send_both, expert_count)
    slot_tokens = recv_both[:, :chunks, :].reshape(slot_total, model_width)
    slot_grads = recv_both[:, chunks:, :].reshape(slot_total, model_width)
    local_in = w_in[0]
    local_down = w_down[0]
    full_in, full_down = (
        lax.all_gather(local_in, "dp", axis=0, tiled=True),
        lax.all_gather(local_down, "dp", axis=0, tiled=True),
    )
    preact = jnp.dot(slot_tokens, full_in, preferred_element_type=jnp.float32)
    grad_hidden = contract_last(slot_grads, full_down)
    pre_grad = pre_grads(preact, grad_hidden)
    slot_back = (
        contract_last(pre_grad, full_in).astype(jnp.bfloat16).reshape(slot_total, chunks, 128)
    )
    hidden_act = hidden_from(preact)
    grad_in_local = lax.psum_scatter(
        contract_first(slot_tokens, pre_grad).astype(jnp.bfloat16),
        "dp",
        scatter_dimension=0,
        tiled=True,
    ).astype(jnp.float32)
    grad_down_local = lax.psum_scatter(
        contract_first(hidden_act, slot_grads).astype(jnp.bfloat16),
        "dp",
        scatter_dimension=0,
        tiled=True,
    ).astype(jnp.float32)
    slot_return = expert_exchange(slot_back, expert_count)
    grad_tokens = (
        contract_first(slot_of_token, slot_return)
        .astype(jnp.bfloat16)
        .reshape(token_rows, model_width)
    )
    return (grad_tokens, grad_in_local[None], grad_down_local[None])


def solution(mesh):
    token_spec = P(("dp", "expert"), None)
    weight_spec = P("expert", "dp", None)
    in_specs = (token_spec, token_spec, token_spec, token_spec, weight_spec, weight_spec)
    out_specs = (token_spec, weight_spec, weight_spec)
    return jax.shard_map(
        on_device, mesh=mesh, in_specs=in_specs, out_specs=out_specs, check_vma=False
    )
```

```python
import jax
import jax.numpy as jnp
from jax import lax
from jax.sharding import PartitionSpec as P


def hidden_from(preact):
    half_width = preact.shape[1] // 2
    gate_pre = preact[:, :half_width]
    up_pre = preact[:, half_width:]
    sigmoid_gate = jax.nn.sigmoid(gate_pre)
    return (gate_pre * sigmoid_gate * up_pre).astype(jnp.bfloat16)


def pre_grads(preact, grad_hidden):
    half_width = preact.shape[1] // 2
    gate_pre = preact[:, :half_width]
    up_pre = preact[:, half_width:]
    sigmoid_gate = jax.nn.sigmoid(gate_pre)
    grad_gate = grad_hidden * up_pre * sigmoid_gate * (1.0 + gate_pre * (1.0 - sigmoid_gate))
    grad_up = grad_hidden * gate_pre * sigmoid_gate
    return jnp.concatenate([grad_gate, grad_up], axis=1).astype(jnp.bfloat16)


def contract_first(left, right):
    return lax.dot_general(
        left, right, (((0,), (0,)), ((), ())), preferred_element_type=jnp.float32
    )


def contract_last(left, right):
    return lax.dot_general(
        left, right, (((1,), (1,)), ((), ())), preferred_element_type=jnp.float32
    )


def expert_exchange(slots, expert_count):
    slot_total, chunks, lanes = slots.shape
    blocks = slots.reshape(expert_count, slot_total // expert_count * chunks, lanes)
    blocks = lax.all_to_all(blocks, "expert", 0, 0, tiled=True)
    return blocks.reshape(slot_total, chunks, lanes)


def on_device(tokens, grad_out, expert_ids, gates, w_in, w_down):
    token_rows, model_width = tokens.shape
    route_width = expert_ids.shape[1]
    expert_count = lax.axis_size("expert")
    route_total = token_rows * route_width
    capacity = route_total // expert_count + max(1, route_total // (8 * expert_count))
    slot_total = expert_count * capacity
    flat_ids = expert_ids.reshape(route_total)
    route_marks = (flat_ids[:, None] == jnp.arange(expert_count, dtype=jnp.int32)[None, :]).astype(
        jnp.int32
    )
    route_index = jnp.arange(route_total, dtype=jnp.int32)
    lower_table = (route_index[None, :] <= route_index[:, None]).astype(jnp.bfloat16)
    running = jnp.dot(
        lower_table, route_marks.astype(jnp.bfloat16), preferred_element_type=jnp.float32
    )
    slot_ranks = jnp.sum((running.astype(jnp.int32) - 1) * route_marks, axis=1)
    targets = flat_ids * capacity + slot_ranks
    slot_index = jnp.arange(slot_total, dtype=jnp.int32)
    slot_hits = slot_index[:, None] == targets[None, :]
    slot_gates = jnp.sum(jnp.where(slot_hits, gates.reshape(route_total)[None, :], 0.0), axis=1)
    token_of_route = (
        route_index[:, None] // route_width == jnp.arange(token_rows, dtype=jnp.int32)[None, :]
    ).astype(jnp.bfloat16)
    slot_of_token = jnp.dot(
        slot_hits.astype(jnp.bfloat16), token_of_route, preferred_element_type=jnp.float32
    ).astype(jnp.bfloat16)
    chunks = model_width // 128
    token_parts = tokens.reshape(token_rows, 1, chunks, 128)
    grad_parts = grad_out.reshape(token_rows, 1, chunks, 128).astype(jnp.float32)
    route_tokens = jnp.broadcast_to(token_parts, (token_rows, route_width, chunks, 128))
    route_grads = (gates[:, :, None, None] * grad_parts).astype(jnp.bfloat16)
    route_rows = jnp.concatenate([route_tokens, route_grads], axis=2).reshape(
        route_total, 2 * chunks, 128
    )
    route_rows = jnp.concatenate(
        [route_rows, jnp.zeros((1, 2 * chunks, 128), jnp.bfloat16)], axis=0
    )
    slot_routes = jnp.sum(jnp.where(slot_hits, route_index[None, :], 0), axis=1)
    occupied = jnp.any(slot_hits, axis=1)
    send_both = route_rows[jnp.where(occupied, slot_routes, route_total)]
    recv_both = expert_exchange(send_both, expert_count)
    slot_tokens = recv_both[:, :chunks, :].reshape(slot_total, model_width)
    slot_grads = recv_both[:, chunks:, :].reshape(slot_total, model_width)
    local_in = w_in[0]
    local_down = w_down[0]
    full_in, full_down = (
        lax.all_gather(local_in, "dp", axis=0, tiled=True),
        lax.all_gather(local_down, "dp", axis=0, tiled=True),
    )
    preact = jnp.dot(slot_tokens, full_in, preferred_element_type=jnp.float32)
    grad_hidden = contract_last(slot_grads, full_down)
    pre_grad = pre_grads(preact, grad_hidden)
    slot_back = (
        contract_last(pre_grad, full_in).astype(jnp.bfloat16).reshape(slot_total, chunks, 128)
    )
    hidden_act = hidden_from(preact)
    grad_in_local = lax.psum_scatter(
        contract_first(slot_tokens, pre_grad).astype(jnp.bfloat16),
        "dp",
        scatter_dimension=0,
        tiled=True,
    ).astype(jnp.float32)
    grad_down_local = lax.psum_scatter(
        contract_first(hidden_act, slot_grads).astype(jnp.bfloat16),
        "dp",
        scatter_dimension=0,
        tiled=True,
    ).astype(jnp.float32)
    slot_return = expert_exchange(slot_back, expert_count)
    grad_tokens = (
        contract_first(slot_of_token, slot_return)
        .astype(jnp.bfloat16)
        .reshape(token_rows, model_width)
    )
    return (grad_tokens, grad_in_local[None], grad_down_local[None])


def solution(mesh):
    token_spec = P(("dp", "expert"), None)
    weight_spec = P("expert", "dp", None)
    in_specs = (token_spec, token_spec, token_spec, token_spec, weight_spec, weight_spec)
    out_specs = (token_spec, weight_spec, weight_spec)
    return jax.shard_map(
        on_device, mesh=mesh, in_specs=in_specs, out_specs=out_specs, check_vma=False
    )
```

```python
import jax
import jax.numpy as jnp
from jax import lax
from jax.sharding import PartitionSpec as P


def hidden_from(preact):
    half_width = preact.shape[1] // 2
    gate_pre = preact[:, :half_width]
    up_pre = preact[:, half_width:]
    sigmoid_gate = jax.nn.sigmoid(gate_pre)
    return (gate_pre * sigmoid_gate * up_pre).astype(jnp.bfloat16)


def pre_grads(preact, grad_hidden):
    half_width = preact.shape[1] // 2
    gate_pre = preact[:, :half_width]
    up_pre = preact[:, half_width:]
    sigmoid_gate = jax.nn.sigmoid(gate_pre)
    grad_gate = grad_hidden * up_pre * sigmoid_gate * (1.0 + gate_pre * (1.0 - sigmoid_gate))
    grad_up = grad_hidden * gate_pre * sigmoid_gate
    return jnp.concatenate([grad_gate, grad_up], axis=1).astype(jnp.bfloat16)


def contract_first(left, right):
    return lax.dot_general(
        left, right, (((0,), (0,)), ((), ())), preferred_element_type=jnp.float32
    )


def contract_last(left, right):
    return lax.dot_general(
        left, right, (((1,), (1,)), ((), ())), preferred_element_type=jnp.float32
    )


def expert_exchange(slots, expert_count):
    slot_total, chunks, lanes = slots.shape
    blocks = slots.reshape(expert_count, slot_total // expert_count * chunks, lanes)
    blocks = lax.all_to_all(blocks, "expert", 0, 0, tiled=True)
    return blocks.reshape(slot_total, chunks, lanes)


def on_device(tokens, grad_out, expert_ids, gates, w_in, w_down):
    token_rows, model_width = tokens.shape
    route_width = expert_ids.shape[1]
    expert_count = lax.axis_size("expert")
    route_total = token_rows * route_width
    capacity = route_total // expert_count + max(1, route_total // (8 * expert_count))
    slot_total = expert_count * capacity
    flat_ids = expert_ids.reshape(route_total)
    route_marks = (flat_ids[:, None] == jnp.arange(expert_count, dtype=jnp.int32)[None, :]).astype(
        jnp.int32
    )
    route_index = jnp.arange(route_total, dtype=jnp.int32)
    lower_table = (route_index[None, :] <= route_index[:, None]).astype(jnp.bfloat16)
    running = jnp.dot(
        lower_table, route_marks.astype(jnp.bfloat16), preferred_element_type=jnp.float32
    )
    slot_ranks = jnp.sum((running.astype(jnp.int32) - 1) * route_marks, axis=1)
    targets = flat_ids * capacity + slot_ranks
    slot_index = jnp.arange(slot_total, dtype=jnp.int32)
    slot_hits = slot_index[:, None] == targets[None, :]
    slot_gates = jnp.sum(jnp.where(slot_hits, gates.reshape(route_total)[None, :], 0.0), axis=1)
    token_of_route = (
        route_index[:, None] // route_width == jnp.arange(token_rows, dtype=jnp.int32)[None, :]
    ).astype(jnp.bfloat16)
    slot_of_token = jnp.dot(
        slot_hits.astype(jnp.bfloat16), token_of_route, preferred_element_type=jnp.float32
    ).astype(jnp.bfloat16)
    chunks = model_width // 128
    both_rows = jnp.concatenate(
        [tokens.reshape(token_rows, chunks, 128), grad_out.reshape(token_rows, chunks, 128)],
        axis=1,
    )
    slot_routes = jnp.sum(jnp.where(slot_hits, route_index[None, :], 0), axis=1)
    occupied = jnp.any(slot_hits, axis=1)
    picked = both_rows[slot_routes // route_width].astype(jnp.float32)
    chunk_index = jnp.arange(2 * chunks, dtype=jnp.int32)[None, :, None]
    row_scale = jnp.where(chunk_index < chunks, jnp.ones((), jnp.float32), slot_gates[:, None, None])
    row_scale = jnp.where(occupied[:, None, None], row_scale, jnp.zeros((), jnp.float32))
    send_both = (row_scale * picked).astype(jnp.bfloat16)
    recv_both = expert_exchange(send_both, expert_count)
    slot_tokens = recv_both[:, :chunks, :].reshape(slot_total, model_width)
    slot_grads = recv_both[:, chunks:, :].reshape(slot_total, model_width)
    local_in = w_in[0]
    local_down = w_down[0]
    full_in, full_down = (
        lax.all_gather(local_in, "dp", axis=0, tiled=True),
        lax.all_gather(local_down, "dp", axis=0, tiled=True),
    )
    preact = jnp.dot(slot_tokens, full_in, preferred_element_type=jnp.float32)
    grad_hidden = contract_last(slot_grads, full_down)
    pre_grad = pre_grads(preact, grad_hidden)
    slot_back = (
        contract_last(pre_grad, full_in).astype(jnp.bfloat16).reshape(slot_total, chunks, 128)
    )
    hidden_act = hidden_from(preact)
    grad_in_local = lax.psum_scatter(
        contract_first(slot_tokens, pre_grad).astype(jnp.bfloat16),
        "dp",
        scatter_dimension=0,
        tiled=True,
    ).astype(jnp.float32)
    grad_down_local = lax.psum_scatter(
        contract_first(hidden_act, slot_grads).astype(jnp.bfloat16),
        "dp",
        scatter_dimension=0,
        tiled=True,
    ).astype(jnp.float32)
    slot_return = expert_exchange(slot_back, expert_count)
    per_route = slot_return[targets].astype(jnp.float32)
    grad_tokens = (
        jnp.sum(per_route.reshape(token_rows, route_width, chunks, 128), axis=1)
        .astype(jnp.bfloat16)
        .reshape(token_rows, model_width)
    )
    return (grad_tokens, grad_in_local[None], grad_down_local[None])


def solution(mesh):
    token_spec = P(("dp", "expert"), None)
    weight_spec = P("expert", "dp", None)
    in_specs = (token_spec, token_spec, token_spec, token_spec, weight_spec, weight_spec)
    out_specs = (token_spec, weight_spec, weight_spec)
    return jax.shard_map(
        on_device, mesh=mesh, in_specs=in_specs, out_specs=out_specs, check_vma=False
    )
```

```python
import jax
import jax.numpy as jnp
from jax import lax
from jax.sharding import PartitionSpec as P


def hidden_from(preact):
    half_width = preact.shape[1] // 2
    gate_pre = preact[:, :half_width]
    up_pre = preact[:, half_width:]
    sigmoid_gate = jax.nn.sigmoid(gate_pre)
    return (gate_pre * sigmoid_gate * up_pre).astype(jnp.bfloat16)


def pre_grads(preact, grad_hidden):
    half_width = preact.shape[1] // 2
    gate_pre = preact[:, :half_width]
    up_pre = preact[:, half_width:]
    sigmoid_gate = jax.nn.sigmoid(gate_pre)
    grad_gate = grad_hidden * up_pre * sigmoid_gate * (1.0 + gate_pre * (1.0 - sigmoid_gate))
    grad_up = grad_hidden * gate_pre * sigmoid_gate
    return jnp.concatenate([grad_gate, grad_up], axis=1).astype(jnp.bfloat16)


def contract_first(left, right):
    return lax.dot_general(
        left, right, (((0,), (0,)), ((), ())), preferred_element_type=jnp.float32
    )


def contract_last(left, right):
    return lax.dot_general(
        left, right, (((1,), (1,)), ((), ())), preferred_element_type=jnp.float32
    )


def expert_exchange(slots, expert_count):
    slot_total, chunks, lanes = slots.shape
    blocks = slots.reshape(expert_count, slot_total // expert_count * chunks, lanes)
    blocks = lax.all_to_all(blocks, "expert", 0, 0, tiled=True)
    return blocks.reshape(slot_total, chunks, lanes)


def on_device(tokens, grad_out, expert_ids, gates, w_in, w_down):
    token_rows, model_width = tokens.shape
    route_width = expert_ids.shape[1]
    expert_count = lax.axis_size("expert")
    route_total = token_rows * route_width
    capacity = route_total // expert_count + max(1, route_total // (8 * expert_count))
    slot_total = expert_count * capacity
    flat_ids = expert_ids.reshape(route_total)
    route_marks = (flat_ids[:, None] == jnp.arange(expert_count, dtype=jnp.int32)[None, :]).astype(
        jnp.int32
    )
    route_index = jnp.arange(route_total, dtype=jnp.int32)
    lower_table = (route_index[None, :] <= route_index[:, None]).astype(jnp.bfloat16)
    running = jnp.dot(
        lower_table, route_marks.astype(jnp.bfloat16), preferred_element_type=jnp.float32
    )
    slot_ranks = jnp.sum((running.astype(jnp.int32) - 1) * route_marks, axis=1)
    targets = flat_ids * capacity + slot_ranks
    slot_index = jnp.arange(slot_total, dtype=jnp.int32)
    slot_hits = slot_index[:, None] == targets[None, :]
    slot_gates = jnp.sum(jnp.where(slot_hits, gates.reshape(route_total)[None, :], 0.0), axis=1)
    token_of_route = (
        route_index[:, None] // route_width == jnp.arange(token_rows, dtype=jnp.int32)[None, :]
    ).astype(jnp.bfloat16)
    slot_of_token = jnp.dot(
        slot_hits.astype(jnp.bfloat16), token_of_route, preferred_element_type=jnp.float32
    ).astype(jnp.bfloat16)
    chunks = model_width // 128
    both_rows = jnp.concatenate(
        [tokens.reshape(token_rows, chunks, 128), grad_out.reshape(token_rows, chunks, 128)],
        axis=1,
    )
    slot_routes = jnp.sum(jnp.where(slot_hits, route_index[None, :], 0), axis=1)
    occupied = jnp.any(slot_hits, axis=1)
    picked = both_rows[slot_routes // route_width]
    picked_grads = picked[:, chunks:, :].astype(jnp.float32)
    send_grads = (slot_gates[:, None, None] * picked_grads).astype(jnp.bfloat16)
    send_tokens = jnp.where(occupied[:, None, None], picked[:, :chunks, :], jnp.zeros((), jnp.bfloat16))
    send_both = jnp.concatenate([send_tokens, send_grads], axis=1)
    recv_both = expert_exchange(send_both, expert_count)
    slot_tokens = recv_both[:, :chunks, :].reshape(slot_total, model_width)
    slot_grads = recv_both[:, chunks:, :].reshape(slot_total, model_width)
    local_in = w_in[0]
    local_down = w_down[0]
    full_in, full_down = (
        lax.all_gather(local_in, "dp", axis=0, tiled=True),
        lax.all_gather(local_down, "dp", axis=0, tiled=True),
    )
    preact = jnp.dot(slot_tokens, full_in, preferred_element_type=jnp.float32)
    grad_hidden = contract_last(slot_grads, full_down)
    pre_grad = pre_grads(preact, grad_hidden)
    slot_back = (
        contract_last(pre_grad, full_in).astype(jnp.bfloat16).reshape(slot_total, chunks, 128)
    )
    hidden_act = hidden_from(preact)
    grad_in_local = lax.psum_scatter(
        contract_first(slot_tokens, pre_grad).astype(jnp.bfloat16),
        "dp",
        scatter_dimension=0,
        tiled=True,
    ).astype(jnp.float32)
    grad_down_local = lax.psum_scatter(
        contract_first(hidden_act, slot_grads).astype(jnp.bfloat16),
        "dp",
        scatter_dimension=0,
        tiled=True,
    ).astype(jnp.float32)
    slot_return = expert_exchange(slot_back, expert_count)
    grad_tokens = (
        contract_first(slot_of_token, slot_return)
        .astype(jnp.bfloat16)
        .reshape(token_rows, model_width)
    )
    return (grad_tokens, grad_in_local[None], grad_down_local[None])


def solution(mesh):
    token_spec = P(("dp", "expert"), None)
    weight_spec = P("expert", "dp", None)
    in_specs = (token_spec, token_spec, token_spec, token_spec, weight_spec, weight_spec)
    out_specs = (token_spec, weight_spec, weight_spec)
    return jax.shard_map(
        on_device, mesh=mesh, in_specs=in_specs, out_specs=out_specs, check_vma=False
    )
```
